512 devices in a mesh: dp: 8 (over z), expert: 64 (over y, x, core).
Axes of the slice: x: 4, y: 8, z: 8, core: 2. Of those that a mesh axis runs over, the one named last changes fastest.
Arguments:
- tokens: bfloat16 [65536, 1024], P(('dp', 'expert')), may hold values from -6 to 6
- expert_ids: int32 [65536, 4], P(('dp', 'expert')), may hold values from 0 to 63, all different within a row; in each aligned block of 128 rows (0 to 127, 128 to 255, ...) at most 16 rows name the same one
- gate_probs: float32 [65536, 4], P(('dp', 'expert')), may hold values from 0.05 to 1
- gate_up: bfloat16 [64, 1024, 768], P('expert', 'dp'), may hold values from -0.1875 to 0.1875
- down_proj: bfloat16 [64, 384, 1024], P('expert', None, 'dp'), may hold values from -0.3125 to 0.3125
- cotangent: bfloat16 [65536, 1024], P(('dp', 'expert')), may hold values from -0.75 to 0.75
Outputs:
- moe_out: bfloat16 [65536, 1024], P(('dp', 'expert'))
- token_grads: bfloat16 [65536, 1024], P(('dp', 'expert'))
- gate_grads: float32 [65536, 4], P(('dp', 'expert'))
- gate_up_grads: float32 [64, 1024, 768], P('expert', 'dp')
- down_grads: float32 [64, 384, 1024], P('expert', None, 'dp')
The draws below stay inside these ranges and needn't reach their ends.
Inputs may be any that keep to these rules, and one draw needn't show every extreme that they name: `expert_ids`: each row names 4 different experts. Among the rows of one device no expert is named more than 16 times, and in every draw some device names some expert exactly 16 times.
All inputs are finite; a program needn't handle non-finite values.
Results may differ from the reference program's by a relative error of at most 0.012.
Values may be sent and summed in bfloat16 or wider, within the bound.
No kernel may reach another device: no remote copies, remote signals or barrier semaphores. Data moves between devices by JAX's collectives and lax.ppermute only.
A program may use at most 64 MiB of HBM per device.

```python
import math
import jax
import jax.numpy as jnp
import numpy as np
from jax import lax

D = 1024
H = 384
TOPK = 4
TOK_DEV = 128
EXPERTS = 64
CAP = 16
TOKENS = 65536
N_DP = 8
N_EXPERT = 64


def levels(own_key, dims, cuts, smallest, top_value):
    gain, own = 1.0, jax.random.fold_in(own_key, 6)
    for axis_at, shards_of in cuts:
        draws = jnp.exp(jax.random.uniform(jax.random.fold_in(own, axis_at), (shards_of,), jnp.float32, smallest / len(cuts), top_value / len(cuts)))
        gain = gain * jnp.repeat(draws, dims[axis_at] // shards_of).reshape([-1 if axis == axis_at else 1 for axis in range(len(dims))])
    return gain


def routed_block(own_key, own, number, rows, amount, top, reach, slope):
    sequence = jax.random.permutation(own_key, amount)
    crowded, ordinary = shares(amount, rows * top, reach, slope, True), shares(amount, rows * top, reach, slope, False)
    places = jnp.arange(amount)

    def named(tallies, offset_by):
        used = int((tallies > 0).sum())
        fixed = max(1, used // 4)
        moved = fixed + (places - fixed + offset_by * (used - fixed)) % max(1, amount - fixed)
        return jnp.zeros((amount,), jnp.int32).at[sequence[jnp.where(places < fixed, places, moved)]].set(jnp.asarray(tallies, jnp.int32))

    tallies = jnp.where(number % 4 == 0, named(crowded, number // 4), named(ordinary, number - number // 4 - 1))
    mixed = jax.random.permutation(jax.random.fold_in(own, 3), amount)
    giver, receiver = mixed[0:amount // 2 * 2:2], mixed[1:amount // 2 * 2:2]
    room = jnp.minimum(tallies[giver] - 1, reach - tallies[receiver]) // 2
    room = jnp.where((giver == sequence[0]) | (receiver == sequence[0]) | (tallies[receiver] == 0), 0, jnp.maximum(room, 0))
    moved = jax.random.randint(jax.random.fold_in(own, 4), (amount // 2,), 0, 1 << 20) % (room + 1)
    tallies = tallies.at[giver].add(-moved).at[receiver].add(moved)
    labels = jnp.searchsorted(jnp.cumsum(tallies), jnp.arange(rows * top), side="right").astype(jnp.int32)
    table = labels.reshape(top, rows).T
    table = table[jax.random.permutation(jax.random.fold_in(own, 1), rows)]
    offset_by = jax.random.randint(jax.random.fold_in(own, 2), (rows, 1), 0, top)
    return jnp.take_along_axis(table, (jnp.arange(top)[None, :] + offset_by) % top, axis=1)


def shares(amount, total, most, skew, full):
    portions = [(1 << 20) // math.isqrt(rank ** skew) + 1 for rank in range(1, amount + 1)]
    largest = most if full else min(most, max(-(-total // amount), total * portions[0] // sum(portions)))
    least = 1 if total - largest >= amount - 1 else 0
    holding, rest = [largest] + [least] * (amount - 1), total - largest - least * (amount - 1)
    while rest > 0:
        movable = [i for i in range(1, amount) if holding[i] < largest] or [i for i in range(1, amount) if holding[i] < most]
        mass, budget = sum([portions[i] for i in movable]), rest
        for i in movable:
            addition = min(most - holding[i], max(1, budget * portions[i] // mass), rest)
            holding[i] = holding[i] + addition
            rest = rest - addition
    return np.array(holding)


def centred(own_key, dims, spread, most, pieces=(), kind=jnp.bfloat16):
    level = levels(own_key, dims, pieces, -0.22, 0.18) if pieces else 1.0
    entries = jax.random.normal(own_key, dims, jnp.float32) * spread * level
    return jnp.minimum(jnp.maximum(entries, -most), most).astype(kind)


def setup_inputs(seed: int = 0) -> dict:
    streams_of = jax.random.split(jax.random.key(seed), 7)
    tokens = centred(streams_of[0], (TOKENS, D), 1.0, 6.0, ((0, 512),))
    expert_ids_keys = jax.random.split(jax.random.fold_in(streams_of[1], 1), TOKENS // TOK_DEV)
    expert_ids_turns = jax.random.permutation(jax.random.fold_in(streams_of[1], 3), TOKENS // TOK_DEV)
    expert_ids = jax.vmap(lambda own, number: routed_block(jax.random.fold_in(streams_of[1], 2), own, number, TOK_DEV, EXPERTS, TOPK, CAP, 3))(expert_ids_keys, expert_ids_turns).reshape((TOKENS, TOPK))
    gate_probs = jnp.clip(0.05 + 0.95 * jax.random.uniform(streams_of[2], (TOKENS, TOPK), jnp.float32) ** levels(streams_of[2], (TOKENS, TOPK), ((0, 512),), -0.2, 0.2), 0.05, 1.0)
    gate_up = centred(streams_of[3], (EXPERTS, D, 2 * H), D ** -0.5, 0.1875, ((0, 64), (1, 8)))
    down_proj = centred(streams_of[4], (EXPERTS, H, D), H ** -0.5, 0.3125, ((0, 64), (2, 8)))
    cotangent = centred(streams_of[5], (TOKENS, D), 0.125, 0.75, ((0, 512),))
    return {"tokens": tokens, "expert_ids": expert_ids, "gate_probs": gate_probs, "gate_up": gate_up, "down_proj": down_proj, "cotangent": cotangent}


def silu_grad(pre_gate, up_value, grad_hidden):
    sigmoid_value = jax.nn.sigmoid(pre_gate)
    grad_gate = grad_hidden * up_value * sigmoid_value * (1.0 + pre_gate * (1.0 - sigmoid_value))
    grad_up = grad_hidden * jax.nn.silu(pre_gate)
    return jnp.concatenate([grad_gate, grad_up], axis=1)

def reference(tokens, expert_ids, gate_probs, gate_up, down_proj, cotangent):
    block_count = N_DP * N_EXPERT
    routes_block = TOK_DEV * TOPK
    group_rows = N_EXPERT * CAP
    routes = expert_ids.reshape(block_count, routes_block)
    expert_range = jnp.arange(EXPERTS, dtype=jnp.int32)
    onehot = (routes[:, :, None] == expert_range[None, None, :]).astype(jnp.int32)
    slot_index = lax.optimization_barrier(jnp.sum((jnp.cumsum(onehot, axis=1) - onehot) * onehot, axis=2)).astype(jnp.int32)
    block_index = jnp.broadcast_to(jnp.arange(block_count, dtype=jnp.int32)[:, None], routes.shape)
    route_index = (block_index * routes_block + jnp.arange(routes_block, dtype=jnp.int32)[None, :]).astype(jnp.int32)
    slot_table = jnp.full((EXPERTS, block_count, CAP), -1, dtype=jnp.int32)
    slot_table = slot_table.at[routes, block_index, slot_index].set(route_index)
    flat_probs = gate_probs.reshape(-1)

    def one_expert(running, inputs):
        out_sum, grad_sum, gate_grad = running
        slot_rows, weight_in, weight_out = inputs
        filled = (slot_rows >= 0).reshape(-1)
        route_of_row = jnp.where(filled, slot_rows.reshape(-1), 0).astype(jnp.int32)
        token_of_row = (route_of_row // TOPK).astype(jnp.int32)
        rows_in = jnp.where(filled[:, None], tokens[token_of_row], jnp.zeros((), tokens.dtype))
        route_probs = jnp.where(filled, flat_probs[route_of_row], 0.0)
        pre_act = jnp.dot(rows_in, weight_in, preferred_element_type=jnp.float32)
        hidden = (jax.nn.silu(pre_act[:, :H]) * pre_act[:, H:]).astype(jnp.bfloat16)
        expert_out = jnp.dot(hidden, weight_out, preferred_element_type=jnp.float32).astype(jnp.bfloat16)
        upstream = cotangent[token_of_row].astype(jnp.float32)
        grad_rows = (route_probs[:, None] * upstream).astype(jnp.bfloat16)
        grad_hidden = jnp.dot(grad_rows, weight_out.T, preferred_element_type=jnp.float32)
        grad_pre = silu_grad(pre_act[:, :H], pre_act[:, H:], grad_hidden).astype(jnp.bfloat16)
        grad_in = jnp.dot(grad_pre, weight_in.T, preferred_element_type=jnp.float32).astype(jnp.bfloat16)
        out_float = expert_out.astype(jnp.float32)
        out_sum = out_sum.at[token_of_row].add(jnp.where(filled[:, None], route_probs[:, None] * out_float, 0.0))
        grad_sum = grad_sum.at[token_of_row].add(jnp.where(filled[:, None], grad_in.astype(jnp.float32), 0.0))
        target = jnp.where(filled, route_of_row, TOKENS * TOPK).astype(jnp.int32)
        gate_grad = gate_grad.at[target].set(lax.optimization_barrier(jnp.sum(upstream * out_float, axis=1)), mode='drop')
        rows_grouped = rows_in.reshape(N_DP, group_rows, D).astype(jnp.float32)
        pre_grouped = grad_pre.reshape(N_DP, group_rows, 2 * H).astype(jnp.float32)
        hidden_grouped = hidden.reshape(N_DP, group_rows, H).astype(jnp.float32)
        grad_grouped = grad_rows.reshape(N_DP, group_rows, D).astype(jnp.float32)
        part_in = jnp.einsum('grd,grh->gdh', rows_grouped, pre_grouped, precision=lax.Precision.HIGHEST)
        part_out = jnp.einsum('grh,grd->ghd', hidden_grouped, grad_grouped, precision=lax.Precision.HIGHEST)
        sum_in = lax.optimization_barrier(jnp.sum(lax.optimization_barrier(part_in.astype(jnp.bfloat16)).astype(jnp.float32), axis=0))
        sum_out = lax.optimization_barrier(jnp.sum(lax.optimization_barrier(part_out.astype(jnp.bfloat16)).astype(jnp.float32), axis=0))
        return ((out_sum, grad_sum, gate_grad), (sum_in, sum_out))
    start_running = (jnp.zeros((TOKENS, D), jnp.float32), jnp.zeros((TOKENS, D), jnp.float32), jnp.zeros((TOKENS * TOPK,), jnp.float32))
    final_running, weight_grads = lax.scan(one_expert, start_running, (slot_table, gate_up, down_proj))
    out_sum, grad_sum, gate_grad = final_running
    gate_up_grads, down_grads = weight_grads
    return (out_sum.astype(jnp.bfloat16), grad_sum.astype(jnp.bfloat16), gate_grad.reshape(TOKENS, TOPK), gate_up_grads, down_grads)
```

```python
import jax
import jax.numpy as jnp
from jax import lax
from jax.sharding import PartitionSpec as P


def expert_rows(rows_in, grad_rows, weight_in, weight_out_t):
    hidden_width = weight_out_t.shape[1]
    contract_last = (((1,), (1,)), ((), ()))
    contract_first = (((0,), (0,)), ((), ()))
    pre_act = jnp.dot(rows_in, weight_in, preferred_element_type=jnp.float32)
    pre_gate = pre_act[:, :hidden_width]
    up_value = pre_act[:, hidden_width:]
    act = jax.nn.silu(pre_gate)
    hidden = (act * up_value).astype(jnp.bfloat16)
    expert_out = lax.dot_general(
        hidden, weight_out_t, contract_last, preferred_element_type=jnp.float32
    ).astype(jnp.bfloat16)
    grad_hidden = jnp.dot(grad_rows, weight_out_t, preferred_element_type=jnp.float32)
    sigmoid_value = jax.nn.sigmoid(pre_gate)
    grad_gate = grad_hidden * up_value * sigmoid_value * (1.0 + pre_gate * (1.0 - sigmoid_value))
    grad_up = grad_hidden * act
    grad_pre = jnp.concatenate([grad_gate, grad_up], axis=1).astype(jnp.bfloat16)
    grad_in = lax.dot_general(
        grad_pre, weight_in, contract_last, preferred_element_type=jnp.float32
    ).astype(jnp.bfloat16)
    weight_in_grad = lax.dot_general(
        rows_in, grad_pre, contract_first, preferred_element_type=jnp.float32
    ).astype(jnp.bfloat16)
    weight_out_grad_t = lax.dot_general(
        grad_rows, hidden, contract_first, preferred_element_type=jnp.float32
    ).astype(jnp.bfloat16)
    return expert_out, grad_in, weight_in_grad, weight_out_grad_t


def local(tokens, expert_ids, gate_probs, gate_up, down_proj, cotangent):
    token_count, top_count = expert_ids.shape
    width = tokens.shape[1]
    expert_count = lax.axis_size("expert")
    capacity = 2 * token_count * top_count // expert_count
    route_count = token_count * top_count
    slot_count = expert_count * capacity
    gate_width = gate_up.shape[2]

    weights = jnp.concatenate([gate_up[0], down_proj[0].T], axis=1)
    weights = lax.all_gather(weights, "dp", axis=0, tiled=True)
    weight_in = weights[:, :gate_width]
    weight_out_t = weights[:, gate_width:]

    flat_ids = expert_ids.reshape(route_count)
    onehot = (flat_ids[:, None] == jnp.arange(expert_count, dtype=jnp.int32)[None, :]).astype(
        jnp.int32
    )
    slot_index = jnp.sum((jnp.cumsum(onehot, axis=0) - onehot) * onehot, axis=1)
    position = (flat_ids * capacity + slot_index).reshape(token_count, top_count)
    slot_range = jnp.arange(slot_count, dtype=jnp.int32)
    hits = position[None, :, :] == slot_range[:, None, None]
    select = jnp.any(hits, axis=2)
    weighted = jnp.sum(jnp.where(hits, gate_probs[None, :, :], 0.0), axis=2)
    slot_probs = jnp.sum(weighted, axis=1)
    select_rows = select.astype(jnp.bfloat16)

    both = jnp.concatenate([tokens, cotangent], axis=1)
    gathered = jnp.dot(select_rows, both, preferred_element_type=jnp.float32)
    send_tokens = gathered[:, :width].astype(jnp.bfloat16)
    slot_cot = gathered[:, width:]
    send_grads = (slot_probs[:, None] * slot_cot).astype(jnp.bfloat16)
    send = jnp.concatenate([send_tokens, send_grads], axis=1)

    recv = lax.all_to_all(send, "expert", split_axis=0, concat_axis=0, tiled=True)
    rows_in = recv[:, :width]
    grad_rows = recv[:, width:]
    expert_out, grad_in, weight_in_grad, weight_out_grad_t = expert_rows(
        rows_in, grad_rows, weight_in, weight_out_t
    )
    back = lax.all_to_all(
        jnp.concatenate([expert_out, grad_in], axis=1),
        "expert",
        split_axis=0,
        concat_axis=0,
        tiled=True,
    )
    grads = lax.psum_scatter(
        jnp.concatenate([weight_in_grad, weight_out_grad_t], axis=1),
        "dp",
        scatter_dimension=0,
        tiled=True,
    ).astype(jnp.float32)
    sum_in = grads[None, :, :gate_width]
    sum_out = grads[:, gate_width:].T[None]

    back_out = back[:, :width].astype(jnp.float32)
    back_grad = back[:, width:]
    moe_out = lax.dot_general(
        weighted,
        back_out,
        (((0,), (0,)), ((), ())),
        precision=lax.Precision.HIGHEST,
        preferred_element_type=jnp.float32,
    ).astype(jnp.bfloat16)
    token_grads = lax.dot_general(
        select_rows, back_grad, (((0,), (0,)), ((), ())), preferred_element_type=jnp.float32
    ).astype(jnp.bfloat16)
    slot_gate = jnp.sum(slot_cot * back_out, axis=1)
    gate_grads = slot_gate[position]
    return (moe_out, token_grads, gate_grads, sum_in, sum_out)


def solution(mesh):
    return jax.shard_map(
        local,
        mesh=mesh,
        in_specs=(
            P(("dp", "expert"), None),
            P(("dp", "expert"), None),
            P(("dp", "expert"), None),
            P("expert", "dp", None),
            P("expert", None, "dp"),
            P(("dp", "expert"), None),
        ),
        out_specs=(
            P(("dp", "expert"), None),
            P(("dp", "expert"), None),
            P(("dp", "expert"), None),
            P("expert", "dp", None),
            P("expert", None, "dp"),
        ),
        check_vma=False,
    )
```

```python
import jax
import jax.numpy as jnp
from jax import lax
from jax.experimental.layout import Layout, with_layout_constraint
from jax.sharding import PartitionSpec as P


def row_major(x):
    return with_layout_constraint(x, Layout(major_to_minor=tuple(range(x.ndim))))


def expert_rows(rows_in, grad_rows, weight_in, weight_out_t):
    hidden_width = weight_out_t.shape[1]
    contract_last = (((1,), (1,)), ((), ()))
    contract_first = (((0,), (0,)), ((), ()))
    pre_act = jnp.dot(rows_in, weight_in, preferred_element_type=jnp.float32)
    pre_gate = pre_act[:, :hidden_width]
    up_value = pre_act[:, hidden_width:]
    act = jax.nn.silu(pre_gate)
    hidden = (act * up_value).astype(jnp.bfloat16)
    expert_out = lax.dot_general(
        hidden, weight_out_t, contract_last, preferred_element_type=jnp.float32
    ).astype(jnp.bfloat16)
    grad_hidden = jnp.dot(grad_rows, weight_out_t, preferred_element_type=jnp.float32)
    sigmoid_value = jax.nn.sigmoid(pre_gate)
    grad_gate = grad_hidden * up_value * sigmoid_value * (1.0 + pre_gate * (1.0 - sigmoid_value))
    grad_up = grad_hidden * act
    grad_pre = jnp.concatenate([grad_gate, grad_up], axis=1).astype(jnp.bfloat16)
    grad_in = lax.dot_general(
        grad_pre, weight_in, contract_last, preferred_element_type=jnp.float32
    ).astype(jnp.bfloat16)
    weight_in_grad = lax.dot_general(
        rows_in, grad_pre, contract_first, preferred_element_type=jnp.float32
    ).astype(jnp.bfloat16)
    weight_out_grad_t = lax.dot_general(
        grad_rows, hidden, contract_first, preferred_element_type=jnp.float32
    ).astype(jnp.bfloat16)
    return expert_out, grad_in, weight_in_grad, weight_out_grad_t


def local(tokens, expert_ids, gate_probs, gate_up, down_proj, cotangent):
    token_count, top_count = expert_ids.shape
    width = tokens.shape[1]
    expert_count = lax.axis_size("expert")
    capacity = 2 * token_count * top_count // expert_count
    route_count = token_count * top_count
    slot_count = expert_count * capacity
    gate_width = gate_up.shape[2]

    weights = jnp.concatenate([gate_up[0], down_proj[0].T], axis=1)
    weights = lax.all_gather(weights, "dp", axis=0, tiled=True)
    weight_in = weights[:, :gate_width]
    weight_out_t = weights[:, gate_width:]

    flat_ids = expert_ids.reshape(route_count)
    onehot = (flat_ids[:, None] == jnp.arange(expert_count, dtype=jnp.int32)[None, :]).astype(
        jnp.int32
    )
    slot_index = jnp.sum((jnp.cumsum(onehot, axis=0) - onehot) * onehot, axis=1)
    position = (flat_ids * capacity + slot_index).reshape(token_count, top_count)
    slot_range = jnp.arange(slot_count, dtype=jnp.int32)
    hits = position[None, :, :] == slot_range[:, None, None]
    select = jnp.any(hits, axis=2)
    weighted = jnp.sum(jnp.where(hits, gate_probs[None, :, :], 0.0), axis=2)
    slot_probs = jnp.sum(weighted, axis=1)
    select_rows = select.astype(jnp.bfloat16)

    both = jnp.concatenate([tokens, cotangent], axis=1)
    gathered = jnp.dot(select_rows, both, preferred_element_type=jnp.bfloat16)
    send_tokens = gathered[:, :width]
    slot_cot = gathered[:, width:]
    send_grads = (slot_probs[:, None] * slot_cot.astype(jnp.float32)).astype(jnp.bfloat16)
    send = jnp.concatenate([send_tokens, send_grads], axis=1)

    recv = lax.all_to_all(send, "expert", split_axis=0, concat_axis=0, tiled=True)
    rows_in = recv[:, :width]
    grad_rows = recv[:, width:]
    expert_out, grad_in, weight_in_grad, weight_out_grad_t = expert_rows(
        rows_in, grad_rows, weight_in, weight_out_t
    )
    back = lax.all_to_all(
        jnp.concatenate([row_major(expert_out), row_major(grad_in)], axis=1),
        "expert",
        split_axis=0,
        concat_axis=0,
        tiled=True,
    )
    grads = lax.psum_scatter(
        jnp.concatenate([weight_in_grad, weight_out_grad_t], axis=1),
        "dp",
        scatter_dimension=0,
        tiled=True,
    ).astype(jnp.float32)
    sum_in = grads[None, :, :gate_width]
    sum_out = grads[:, gate_width:].T[None]

    back_out = back[:, :width].astype(jnp.float32)
    back_grad = back[:, width:]
    moe_out = lax.dot_general(
        weighted,
        back_out,
        (((0,), (0,)), ((), ())),
        precision=lax.Precision.HIGHEST,
        preferred_element_type=jnp.float32,
    ).astype(jnp.bfloat16)
    token_grads = lax.dot_general(
        select_rows, back_grad, (((0,), (0,)), ((), ())), preferred_element_type=jnp.float32
    ).astype(jnp.bfloat16)
    slot_gate = jnp.sum(slot_cot.astype(jnp.float32) * back_out, axis=1)
    gate_grads = jnp.sum(jnp.where(hits, slot_gate[:, None, None], 0.0), axis=0)
    return (moe_out, token_grads, gate_grads, sum_in, sum_out)


def solution(mesh):
    return jax.shard_map(
        local,
        mesh=mesh,
        in_specs=(
            P(("dp", "expert"), None),
            P(("dp", "expert"), None),
            P(("dp", "expert"), None),
            P("expert", "dp", None),
            P("expert", None, "dp"),
            P(("dp", "expert"), None),
        ),
        out_specs=(
            P(("dp", "expert"), None),
            P(("dp", "expert"), None),
            P(("dp", "expert"), None),
            P("expert", "dp", None),
            P("expert", None, "dp"),
        ),
        check_vma=False,
    )
```

```python
import jax
import jax.numpy as jnp
from jax import lax
from jax.experimental.layout import Layout, with_layout_constraint
from jax.sharding import PartitionSpec as P


def row_major(x):
    return with_layout_constraint(x, Layout(major_to_minor=tuple(range(x.ndim))))


def expert_rows(rows_in, grad_rows, weight_in, weight_out_t):
    hidden_width = weight_out_t.shape[1]
    contract_last = (((1,), (1,)), ((), ()))
    contract_first = (((0,), (0,)), ((), ()))
    pre_act = jnp.dot(rows_in, weight_in, preferred_element_type=jnp.float32)
    pre_gate = pre_act[:, :hidden_width]
    up_value = pre_act[:, hidden_width:]
    act = jax.nn.silu(pre_gate)
    hidden = (act * up_value).astype(jnp.bfloat16)
    expert_out = lax.dot_general(
        hidden, weight_out_t, contract_last, preferred_element_type=jnp.float32
    ).astype(jnp.bfloat16)
    grad_hidden = jnp.dot(grad_rows, weight_out_t, preferred_element_type=jnp.float32)
    sigmoid_value = jax.nn.sigmoid(pre_gate)
    grad_gate = grad_hidden * up_value * sigmoid_value * (1.0 + pre_gate * (1.0 - sigmoid_value))
    grad_up = grad_hidden * act
    grad_pre = jnp.concatenate([grad_gate, grad_up], axis=1).astype(jnp.bfloat16)
    grad_in = lax.dot_general(
        grad_pre, weight_in, contract_last, preferred_element_type=jnp.float32
    ).astype(jnp.bfloat16)
    weight_in_grad = lax.dot_general(
        rows_in, grad_pre, contract_first, preferred_element_type=jnp.float32
    ).astype(jnp.bfloat16)
    weight_out_grad_t = lax.dot_general(
        grad_rows, hidden, contract_first, preferred_element_type=jnp.float32
    ).astype(jnp.bfloat16)
    return expert_out, grad_in, weight_in_grad, weight_out_grad_t


def gather_dp(block):
    size = lax.axis_size("dp")
    me = lax.axis_index("dp")
    pieces = [block]
    for shift in range(1, size):
        pairs = [(i, (i + shift) % size) for i in range(size)]
        pieces.append(lax.ppermute(block, "dp", pairs))
    stacked = jnp.stack(pieces[::-1] + pieces[::-1])
    return lax.dynamic_slice_in_dim(stacked, size - 1 - me, size, axis=0).reshape(
        size * block.shape[0], block.shape[1]
    )


def scatter_dp(full):
    size = lax.axis_size("dp")
    me = lax.axis_index("dp")
    rows = full.shape[0] // size
    blocks = full.reshape(size, rows, full.shape[1])
    total = lax.dynamic_index_in_dim(blocks, me, axis=0, keepdims=False).astype(jnp.float32)
    for shift in range(1, size):
        pairs = [(i, (i + shift) % size) for i in range(size)]
        part = lax.dynamic_index_in_dim(blocks, (me + shift) % size, axis=0, keepdims=False)
        total = total + lax.ppermute(part, "dp", pairs).astype(jnp.float32)
    return total


def local(tokens, expert_ids, gate_probs, gate_up, down_proj, cotangent):
    token_count, top_count = expert_ids.shape
    width = tokens.shape[1]
    expert_count = lax.axis_size("expert")
    capacity = 2 * token_count * top_count // expert_count
    route_count = token_count * top_count
    slot_count = expert_count * capacity
    gate_width = gate_up.shape[2]

    weights = gather_dp(jnp.concatenate([gate_up[0], down_proj[0].T], axis=1))
    weight_in = weights[:, :gate_width]
    weight_out_t = weights[:, gate_width:]

    flat_ids = expert_ids.reshape(route_count)
    onehot = (flat_ids[:, None] == jnp.arange(expert_count, dtype=jnp.int32)[None, :]).astype(
        jnp.int32
    )
    slot_index = jnp.sum((jnp.cumsum(onehot, axis=0) - onehot) * onehot, axis=1)
    position = (flat_ids * capacity + slot_index).reshape(token_count, top_count)
    slot_range = jnp.arange(slot_count, dtype=jnp.int32)
    hits = position[None, :, :] == slot_range[:, None, None]
    select = jnp.any(hits, axis=2)
    weighted = jnp.sum(jnp.where(hits, gate_probs[None, :, :], 0.0), axis=2)
    slot_probs = jnp.sum(weighted, axis=1)
    select_rows = select.astype(jnp.bfloat16)

    both = jnp.concatenate([tokens, cotangent], axis=1)
    gathered = jnp.dot(select_rows, both, preferred_element_type=jnp.float32)
    column = lax.broadcasted_iota(jnp.int32, gathered.shape, 1)
    send = (gathered * jnp.where(column < width, 1.0, slot_probs[:, None])).astype(jnp.bfloat16)

    recv = lax.all_to_all(send, "expert", split_axis=0, concat_axis=0, tiled=True)
    rows_in = recv[:, :width]
    grad_rows = recv[:, width:]
    expert_out, grad_in, weight_in_grad, weight_out_grad_t = expert_rows(
        rows_in, grad_rows, weight_in, weight_out_t
    )
    back = lax.all_to_all(
        jnp.concatenate([row_major(expert_out), row_major(grad_in)], axis=1),
        "expert",
        split_axis=0,
        concat_axis=0,
        tiled=True,
    )
    grads = scatter_dp(jnp.concatenate([weight_in_grad, weight_out_grad_t], axis=1))
    sum_in = grads[None, :, :gate_width]
    sum_out = grads[:, gate_width:].T[None]

    back_out = back[:, :width].astype(jnp.float32)
    back_grad = back[:, width:]
    moe_out = lax.dot_general(
        weighted,
        back_out,
        (((0,), (0,)), ((), ())),
        precision=lax.Precision.HIGHEST,
        preferred_element_type=jnp.float32,
    ).astype(jnp.bfloat16)
    token_grads = lax.dot_general(
        select_rows, back_grad, (((0,), (0,)), ((), ())), preferred_element_type=jnp.float32
    ).astype(jnp.bfloat16)
    token_slot = lax.dot_general(
        cotangent, back[:, :width], (((1,), (1,)), ((), ())), preferred_element_type=jnp.float32
    )
    gate_grads = jnp.sum(jnp.where(hits, token_slot.T[:, :, None], 0.0), axis=0)
    return (moe_out, token_grads, gate_grads, sum_in, sum_out)


def solution(mesh):
    return jax.shard_map(
        local,
        mesh=mesh,
        in_specs=(
            P(("dp", "expert"), None),
            P(("dp", "expert"), None),
            P(("dp", "expert"), None),
            P("expert", "dp", None),
            P("expert", None, "dp"),
            P(("dp", "expert"), None),
        ),
        out_specs=(
            P(("dp", "expert"), None),
            P(("dp", "expert"), None),
            P(("dp", "expert"), None),
            P("expert", "dp", None),
            P("expert", None, "dp"),
        ),
        check_vma=False,
    )
```

```python
import jax
import jax.numpy as jnp
from jax import lax
from jax.experimental.layout import Layout, with_layout_constraint
from jax.sharding import PartitionSpec as P


def row_major(x):
    return with_layout_constraint(x, Layout(major_to_minor=tuple(range(x.ndim))))


def expert_rows(rows_in, grad_rows, weight_in, weight_out_t):
    hidden_width = weight_out_t.shape[1]
    contract_last = (((1,), (1,)), ((), ()))
    contract_first = (((0,), (0,)), ((), ()))
    pre_act = jnp.dot(rows_in, weight_in, preferred_element_type=jnp.float32)
    pre_gate = pre_act[:, :hidden_width]
    up_value = pre_act[:, hidden_width:]
    act = jax.nn.silu(pre_gate)
    hidden = (act * up_value).astype(jnp.bfloat16)
    expert_out = lax.dot_general(
        hidden, weight_out_t, contract_last, preferred_element_type=jnp.float32
    ).astype(jnp.bfloat16)
    grad_hidden = jnp.dot(grad_rows, weight_out_t, preferred_element_type=jnp.float32)
    sigmoid_value = jax.nn.sigmoid(pre_gate)
    grad_gate = grad_hidden * up_value * sigmoid_value * (1.0 + pre_gate * (1.0 - sigmoid_value))
    grad_up = grad_hidden * act
    grad_pre = jnp.concatenate([grad_gate, grad_up], axis=1).astype(jnp.bfloat16)
    grad_in = lax.dot_general(
        grad_pre, weight_in, contract_last, preferred_element_type=jnp.float32
    ).astype(jnp.bfloat16)
    weight_in_grad = lax.dot_general(
        rows_in, grad_pre, contract_first, preferred_element_type=jnp.float32
    ).astype(jnp.bfloat16)
    weight_out_grad_t = lax.dot_general(
        grad_rows, hidden, contract_first, preferred_element_type=jnp.float32
    ).astype(jnp.bfloat16)
    return expert_out, grad_in, weight_in_grad, weight_out_grad_t


def gather_dp(block):
    size = lax.axis_size("dp")
    me = lax.axis_index("dp")
    pieces = [block]
    for shift in range(1, size):
        pairs = [(i, (i + shift) % size) for i in range(size)]
        pieces.append(lax.ppermute(block, "dp", pairs))
    stacked = jnp.stack(pieces[::-1] + pieces[::-1])
    return lax.dynamic_slice_in_dim(stacked, size - 1 - me, size, axis=0).reshape(
        size * block.shape[0], block.shape[1]
    )


def scatter_dp(full):
    size = lax.axis_size("dp")
    me = lax.axis_index("dp")
    rows = full.shape[0] // size
    blocks = full.reshape(size, rows, full.shape[1])
    total = lax.dynamic_index_in_dim(blocks, me, axis=0, keepdims=False).astype(jnp.float32)
    for shift in range(1, size):
        pairs = [(i, (i + shift) % size) for i in range(size)]
        part = lax.dynamic_index_in_dim(blocks, (me + shift) % size, axis=0, keepdims=False)
        total = total + lax.ppermute(part, "dp", pairs).astype(jnp.float32)
    return total


def local(tokens, expert_ids, gate_probs, gate_up, down_proj, cotangent):
    token_count, top_count = expert_ids.shape
    width = tokens.shape[1]
    expert_count = lax.axis_size("expert")
    capacity = 2 * token_count * top_count // expert_count
    route_count = token_count * top_count
    slot_count = expert_count * capacity
    gate_width = gate_up.shape[2]

    weights = gather_dp(jnp.concatenate([gate_up[0], down_proj[0].T], axis=1))
    weight_in = weights[:, :gate_width]
    weight_out_t = weights[:, gate_width:]

    flat_ids = expert_ids.reshape(route_count)
    onehot = (flat_ids[:, None] == jnp.arange(expert_count, dtype=jnp.int32)[None, :]).astype(
        jnp.int32
    )
    slot_index = jnp.sum((jnp.cumsum(onehot, axis=0) - onehot) * onehot, axis=1)
    position = (flat_ids * capacity + slot_index).reshape(token_count, top_count)
    slot_range = jnp.arange(slot_count, dtype=jnp.int32)
    hits = position[None, :, :] == slot_range[:, None, None]
    select = jnp.any(hits, axis=2)
    weighted = jnp.sum(jnp.where(hits, gate_probs[None, :, :], 0.0), axis=2)
    slot_probs = jnp.sum(weighted, axis=1)
    select_rows = select.astype(jnp.bfloat16)

    both = jnp.concatenate([tokens, cotangent], axis=1)
    gathered = jnp.dot(select_rows, both, preferred_element_type=jnp.float32)
    column = lax.broadcasted_iota(jnp.int32, gathered.shape, 1)
    send = (gathered * jnp.where(column < width, 1.0, slot_probs[:, None])).astype(jnp.bfloat16)

    recv = lax.all_to_all(send, "expert", split_axis=0, concat_axis=0, tiled=True)
    rows_in = recv[:, :width]
    grad_rows = recv[:, width:]
    expert_out, grad_in, weight_in_grad, weight_out_grad_t = expert_rows(
        rows_in, grad_rows, weight_in, weight_out_t
    )
    back = lax.all_to_all(
        jnp.concatenate([row_major(expert_out), row_major(grad_in)], axis=1),
        "expert",
        split_axis=0,
        concat_axis=0,
        tiled=True,
    )
    grads = scatter_dp(jnp.concatenate([weight_in_grad, weight_out_grad_t], axis=1))
    sum_in = grads[None, :, :gate_width]
    sum_out = grads[:, gate_width:].T[None]

    high = lax.reduce_precision(weighted, exponent_bits=8, mantissa_bits=7)
    rest = weighted - high
    middle = lax.reduce_precision(rest, exponent_bits=8, mantissa_bits=7)
    low = rest - middle
    parts = [part.astype(jnp.bfloat16) for part in (high, middle, low)]
    combine = jnp.concatenate(parts + [select_rows], axis=1)
    summed = lax.dot_general(
        combine, back, (((0,), (0,)), ((), ())), preferred_element_type=jnp.float32
    )
    moe_out = (
        summed[:token_count, :width]
        + summed[token_count : 2 * token_count, :width]
        + summed[2 * token_count : 3 * token_count, :width]
    ).astype(jnp.bfloat16)
    token_grads = summed[3 * token_count :, width:].astype(jnp.bfloat16)
    token_slot = lax.dot_general(
        cotangent, back[:, :width], (((1,), (1,)), ((), ())), preferred_element_type=jnp.float32
    )
    gate_grads = jnp.sum(jnp.where(hits, token_slot.T[:, :, None], 0.0), axis=0)
    return (moe_out, token_grads, gate_grads, sum_in, sum_out)


def solution(mesh):
    return jax.shard_map(
        local,
        mesh=mesh,
        in_specs=(
            P(("dp", "expert"), None),
            P(("dp", "expert"), None),
            P(("dp", "expert"), None),
            P("expert", "dp", None),
            P("expert", None, "dp"),
            P(("dp", "expert"), None),
        ),
        out_specs=(
            P(("dp", "expert"), None),
            P(("dp", "expert"), None),
            P(("dp", "expert"), None),
            P("expert", "dp", None),
            P("expert", None, "dp"),
        ),
        check_vma=False,
    )
```

```python
import jax
import jax.numpy as jnp
from jax import lax
from jax.experimental.layout import Layout, with_layout_constraint
from jax.sharding import PartitionSpec as P


def row_major(x):
    return with_layout_constraint(x, Layout(major_to_minor=tuple(range(x.ndim))))


def expert_rows(rows_in, grad_rows, weight_in, weight_out_t):
    hidden_width = weight_out_t.shape[1]
    contract_last = (((1,), (1,)), ((), ()))
    contract_first = (((0,), (0,)), ((), ()))
    pre_act = row_major(jnp.dot(rows_in, weight_in, preferred_element_type=jnp.float32))
    pre_gate = pre_act[:, :hidden_width]
    up_value = pre_act[:, hidden_width:]
    act = jax.nn.silu(pre_gate)
    hidden = (act * up_value).astype(jnp.bfloat16)
    expert_out = lax.dot_general(
        hidden, weight_out_t, contract_last, preferred_element_type=jnp.float32
    ).astype(jnp.bfloat16)
    grad_hidden = jnp.dot(grad_rows, weight_out_t, preferred_element_type=jnp.float32)
    sigmoid_value = jax.nn.sigmoid(pre_gate)
    grad_gate = grad_hidden * up_value * sigmoid_value * (1.0 + pre_gate * (1.0 - sigmoid_value))
    grad_up = grad_hidden * act
    grad_pre = jnp.concatenate([grad_gate, grad_up], axis=1).astype(jnp.bfloat16)
    grad_in = lax.dot_general(
        grad_pre, weight_in, contract_last, preferred_element_type=jnp.float32
    ).astype(jnp.bfloat16)
    weight_in_grad = lax.dot_general(
        rows_in, grad_pre, contract_first, preferred_element_type=jnp.float32
    ).astype(jnp.bfloat16)
    weight_out_grad_t = lax.dot_general(
        grad_rows, hidden, contract_first, preferred_element_type=jnp.float32
    ).astype(jnp.bfloat16)
    return expert_out, grad_in, weight_in_grad, weight_out_grad_t


def gather_dp(block):
    size = lax.axis_size("dp")
    me = lax.axis_index("dp")
    pieces = [block]
    for shift in range(1, size):
        pairs = [(i, (i + shift) % size) for i in range(size)]
        pieces.append(lax.ppermute(block, "dp", pairs))
    stacked = jnp.stack(pieces[::-1] + pieces[::-1])
    return lax.dynamic_slice_in_dim(stacked, size - 1 - me, size, axis=0).reshape(
        size * block.shape[0], block.shape[1]
    )


def scatter_dp(full):
    size = lax.axis_size("dp")
    me = lax.axis_index("dp")
    rows = full.shape[0] // size
    blocks = full.reshape(size, rows, full.shape[1])
    total = lax.dynamic_index_in_dim(blocks, me, axis=0, keepdims=False).astype(jnp.float32)
    for shift in range(1, size):
        pairs = [(i, (i + shift) % size) for i in range(size)]
        part = lax.dynamic_index_in_dim(blocks, (me + shift) % size, axis=0, keepdims=False)
        total = total + lax.ppermute(part, "dp", pairs).astype(jnp.float32)
    return total


def local(tokens, expert_ids, gate_probs, gate_up, down_proj, cotangent):
    token_count, top_count = expert_ids.shape
    width = tokens.shape[1]
    expert_count = lax.axis_size("expert")
    capacity = 2 * token_count * top_count // expert_count
    route_count = token_count * top_count
    slot_count = expert_count * capacity
    gate_width = gate_up.shape[2]

    weights = gather_dp(jnp.concatenate([gate_up[0], down_proj[0].T], axis=1))
    weight_in = weights[:, :gate_width]
    weight_out_t = weights[:, gate_width:]

    flat_ids = expert_ids.reshape(route_count)
    onehot = (flat_ids[:, None] == jnp.arange(expert_count, dtype=jnp.int32)[None, :]).astype(
        jnp.int32
    )
    slot_index = jnp.sum((jnp.cumsum(onehot, axis=0) - onehot) * onehot, axis=1)
    position = (flat_ids * capacity + slot_index).reshape(token_count, top_count)
    slot_range = jnp.arange(slot_count, dtype=jnp.int32)
    hits = position[None, :, :] == slot_range[:, None, None]
    select = jnp.any(hits, axis=2)
    weighted = jnp.sum(jnp.where(hits, gate_probs[None, :, :], 0.0), axis=2)
    slot_probs = jnp.sum(weighted, axis=1)
    select_rows = select.astype(jnp.bfloat16)

    both = jnp.concatenate([tokens, cotangent], axis=1)
    gathered = jnp.dot(select_rows, both, preferred_element_type=jnp.float32)
    column = lax.broadcasted_iota(jnp.int32, gathered.shape, 1)
    send = (gathered * jnp.where(column < width, 1.0, slot_probs[:, None])).astype(jnp.bfloat16)

    recv = lax.all_to_all(send, "expert", split_axis=0, concat_axis=0, tiled=True)
    rows_in = recv[:, :width]
    grad_rows = recv[:, width:]
    expert_out, grad_in, weight_in_grad, weight_out_grad_t = expert_rows(
        rows_in, grad_rows, weight_in, weight_out_t
    )
    back = lax.all_to_all(
        jnp.concatenate([row_major(expert_out), row_major(grad_in)], axis=1),
        "expert",
        split_axis=0,
        concat_axis=0,
        tiled=True,
    )
    grads = scatter_dp(jnp.concatenate([weight_in_grad, weight_out_grad_t], axis=1))
    sum_in = grads[None, :, :gate_width]
    sum_out = grads[:, gate_width:].T[None]

    high = lax.reduce_precision(weighted, exponent_bits=8, mantissa_bits=7)
    rest = weighted - high
    middle = lax.reduce_precision(rest, exponent_bits=8, mantissa_bits=7)
    low = rest - middle
    parts = [part.astype(jnp.bfloat16) for part in (high, middle, low)]
    combine = jnp.concatenate(parts + [select_rows], axis=1)
    summed = lax.dot_general(
        combine, back, (((0,), (0,)), ((), ())), preferred_element_type=jnp.float32
    )
    moe_out = (
        summed[:token_count, :width]
        + summed[token_count : 2 * token_count, :width]
        + summed[2 * token_count : 3 * token_count, :width]
    ).astype(jnp.bfloat16)
    token_grads = summed[3 * token_count :, width:].astype(jnp.bfloat16)
    token_slot = lax.dot_general(
        cotangent, back[:, :width], (((1,), (1,)), ((), ())), preferred_element_type=jnp.float32
    )
    gate_grads = jnp.sum(jnp.where(hits, token_slot.T[:, :, None], 0.0), axis=0)
    return (moe_out, token_grads, gate_grads, sum_in, sum_out)


def solution(mesh):
    return jax.shard_map(
        local,
        mesh=mesh,
        in_specs=(
            P(("dp", "expert"), None),
            P(("dp", "expert"), None),
            P(("dp", "expert"), None),
            P("expert", "dp", None),
            P("expert", None, "dp"),
            P(("dp", "expert"), None),
        ),
        out_specs=(
            P(("dp", "expert"), None),
            P(("dp", "expert"), None),
            P(("dp", "expert"), None),
            P("expert", "dp", None),
            P("expert", None, "dp"),
        ),
        check_vma=False,
    )
```

```python
import functools

import jax
import jax.numpy as jnp
from jax import lax
from jax.experimental import pallas as pl
from jax.sharding import PartitionSpec as P


def expert_kernel(recv_ref, w_ref, out_ref, hid_ref, dp_ref, *, width, gate_width, hidden_width):
    contract_last = (((1,), (1,)), ((), ()))
    rows = recv_ref[:, :width]
    grads = recv_ref[:, width:]
    w_in = w_ref[:, :gate_width]
    w_out_t = w_ref[:, gate_width:]
    pre = jnp.dot(rows, w_in, preferred_element_type=jnp.float32)
    pre_gate = pre[:, :hidden_width]
    up = pre[:, hidden_width:]
    sig = 1.0 / (1.0 + jnp.exp(-pre_gate))
    act = pre_gate * sig
    hid = (act * up).astype(jnp.bfloat16)
    q = jnp.dot(grads, w_out_t, preferred_element_type=jnp.float32)
    grad_gate = q * up * sig * (1.0 + pre_gate * (1.0 - sig))
    grad_up = q * act
    dp = jnp.concatenate([grad_gate, grad_up], axis=1).astype(jnp.bfloat16)
    out_ref[:, :width] = lax.dot_general(
        hid, w_out_t, contract_last, preferred_element_type=jnp.float32
    ).astype(jnp.bfloat16)
    out_ref[:, width:] = lax.dot_general(
        dp, w_in, contract_last, preferred_element_type=jnp.float32
    ).astype(jnp.bfloat16)
    hid_ref[...] = hid
    dp_ref[...] = dp


def expert_call(recv, weights, gate_width, block=256):
    slots, both = recv.shape
    width = both // 2
    hidden_width = weights.shape[1] - gate_width
    kernel = functools.partial(
        expert_kernel, width=width, gate_width=gate_width, hidden_width=hidden_width
    )
    return pl.pallas_call(
        kernel,
        grid=(slots // block,),
        in_specs=[
            pl.BlockSpec((block, both), lambda i: (i, 0)),
            pl.BlockSpec(weights.shape, lambda i: (0, 0)),
        ],
        out_specs=[
            pl.BlockSpec((block, both), lambda i: (i, 0)),
            pl.BlockSpec((block, hidden_width), lambda i: (i, 0)),
            pl.BlockSpec((block, gate_width), lambda i: (i, 0)),
        ],
        out_shape=[
            jax.ShapeDtypeStruct((slots, both), jnp.bfloat16),
            jax.ShapeDtypeStruct((slots, hidden_width), jnp.bfloat16),
            jax.ShapeDtypeStruct((slots, gate_width), jnp.bfloat16),
        ],
    )(recv, weights)


def gather_dp(block):
    size = lax.axis_size("dp")
    me = lax.axis_index("dp")
    pieces = [block]
    for shift in range(1, size):
        pairs = [(i, (i + shift) % size) for i in range(size)]
        pieces.append(lax.ppermute(block, "dp", pairs))
    stacked = jnp.stack(pieces[::-1] + pieces[::-1])
    return lax.dynamic_slice_in_dim(stacked, size - 1 - me, size, axis=0).reshape(
        size * block.shape[0], block.shape[1]
    )


def scatter_dp(full):
    size = lax.axis_size("dp")
    me = lax.axis_index("dp")
    rows = full.shape[0] // size
    blocks = full.reshape(size, rows, full.shape[1])
    total = lax.dynamic_index_in_dim(blocks, me, axis=0, keepdims=False).astype(jnp.float32)
    for shift in range(1, size):
        pairs = [(i, (i + shift) % size) for i in range(size)]
        part = lax.dynamic_index_in_dim(blocks, (me + shift) % size, axis=0, keepdims=False)
        total = total + lax.ppermute(part, "dp", pairs).astype(jnp.float32)
    return total


def local(tokens, expert_ids, gate_probs, gate_up, down_proj, cotangent):
    token_count, top_count = expert_ids.shape
    width = tokens.shape[1]
    expert_count = lax.axis_size("expert")
    capacity = 2 * token_count * top_count // expert_count
    route_count = token_count * top_count
    slot_count = expert_count * capacity
    gate_width = gate_up.shape[2]

    weights = gather_dp(jnp.concatenate([gate_up[0], down_proj[0].T], axis=1))

    flat_ids = expert_ids.reshape(route_count)
    onehot = (flat_ids[:, None] == jnp.arange(expert_count, dtype=jnp.int32)[None, :]).astype(
        jnp.int32
    )
    slot_index = jnp.sum((jnp.cumsum(onehot, axis=0) - onehot) * onehot, axis=1)
    position = (flat_ids * capacity + slot_index).reshape(token_count, top_count)
    slot_range = jnp.arange(slot_count, dtype=jnp.int32)
    hits = position[None, :, :] == slot_range[:, None, None]
    select = jnp.any(hits, axis=2)
    weighted = jnp.sum(jnp.where(hits, gate_probs[None, :, :], 0.0), axis=2)
    slot_probs = jnp.sum(weighted, axis=1)
    select_rows = select.astype(jnp.bfloat16)

    both = jnp.concatenate([tokens, cotangent], axis=1)
    gathered = jnp.dot(select_rows, both, preferred_element_type=jnp.float32)
    column = lax.broadcasted_iota(jnp.int32, gathered.shape, 1)
    send = (gathered * jnp.where(column < width, 1.0, slot_probs[:, None])).astype(jnp.bfloat16)

    recv = lax.all_to_all(send, "expert", split_axis=0, concat_axis=0, tiled=True)
    payload, hidden, grad_pre = expert_call(recv, weights, gate_width)
    back = lax.all_to_all(payload, "expert", split_axis=0, concat_axis=0, tiled=True)
    contract_first = (((0,), (0,)), ((), ()))
    weight_in_grad = lax.dot_general(
        recv[:, :width], grad_pre, contract_first, preferred_element_type=jnp.float32
    ).astype(jnp.bfloat16)
    weight_out_grad_t = lax.dot_general(
        recv[:, width:], hidden, contract_first, preferred_element_type=jnp.float32
    ).astype(jnp.bfloat16)
    grads = scatter_dp(jnp.concatenate([weight_in_grad, weight_out_grad_t], axis=1))
    sum_in = grads[None, :, :gate_width]
    sum_out = grads[:, gate_width:].T[None]

    high = lax.reduce_precision(weighted, exponent_bits=8, mantissa_bits=7)
    rest = weighted - high
    middle = lax.reduce_precision(rest, exponent_bits=8, mantissa_bits=7)
    low = rest - middle
    parts = [part.astype(jnp.bfloat16) for part in (high, middle, low)]
    combine = jnp.concatenate(parts + [select_rows], axis=1)
    summed = lax.dot_general(
        combine, back, (((0,), (0,)), ((), ())), preferred_element_type=jnp.float32
    )
    moe_out = (
        summed[:token_count, :width]
        + summed[token_count : 2 * token_count, :width]
        + summed[2 * token_count : 3 * token_count, :width]
    ).astype(jnp.bfloat16)
    token_grads = summed[3 * token_count :, width:].astype(jnp.bfloat16)
    token_slot = lax.dot_general(
        cotangent, back[:, :width], (((1,), (1,)), ((), ())), preferred_element_type=jnp.float32
    )
    gate_grads = jnp.sum(jnp.where(hits, token_slot.T[:, :, None], 0.0), axis=0)
    return (moe_out, token_grads, gate_grads, sum_in, sum_out)


def solution(mesh):
    return jax.shard_map(
        local,
        mesh=mesh,
        in_specs=(
            P(("dp", "expert"), None),
            P(("dp", "expert"), None),
            P(("dp", "expert"), None),
            P("expert", "dp", None),
            P("expert", None, "dp"),
            P(("dp", "expert"), None),
        ),
        out_specs=(
            P(("dp", "expert"), None),
            P(("dp", "expert"), None),
            P(("dp", "expert"), None),
            P("expert", "dp", None),
            P("expert", None, "dp"),
        ),
        check_vma=False,
    )
```

```python
import functools

import jax
import jax.numpy as jnp
from jax import lax
from jax.experimental import pallas as pl
from jax.sharding import PartitionSpec as P


def expert_kernel(recv_ref, w_ref, out_ref, hid_ref, dp_ref, *, width, gate_width, hidden_width):
    contract_last = (((1,), (1,)), ((), ()))
    rows = recv_ref[:, :width]
    grads = recv_ref[:, width:]
    w_in = w_ref[:, :gate_width]
    w_out_t = w_ref[:, gate_width:]
    pre = jnp.dot(rows, w_in, preferred_element_type=jnp.float32)
    pre_gate = pre[:, :hidden_width]
    up = pre[:, hidden_width:]
    sig = 1.0 / (1.0 + jnp.exp(-pre_gate))
    act = pre_gate * sig
    hid = (act * up).astype(jnp.bfloat16)
    q = jnp.dot(grads, w_out_t, preferred_element_type=jnp.float32)
    grad_gate = q * up * sig * (1.0 + pre_gate * (1.0 - sig))
    grad_up = q * act
    dp = jnp.concatenate([grad_gate, grad_up], axis=1).astype(jnp.bfloat16)
    out_ref[:, :width] = lax.dot_general(
        hid, w_out_t, contract_last, preferred_element_type=jnp.float32
    ).astype(jnp.bfloat16)
    out_ref[:, width:] = lax.dot_general(
        dp, w_in, contract_last, preferred_element_type=jnp.float32
    ).astype(jnp.bfloat16)
    hid_ref[...] = hid
    dp_ref[...] = dp


def expert_call(recv, weights, gate_width, block=256):
    slots, both = recv.shape
    width = both // 2
    hidden_width = weights.shape[1] - gate_width
    kernel = functools.partial(
        expert_kernel, width=width, gate_width=gate_width, hidden_width=hidden_width
    )
    return pl.pallas_call(
        kernel,
        grid=(slots // block,),
        in_specs=[
            pl.BlockSpec((block, both), lambda i: (i, 0)),
            pl.BlockSpec(weights.shape, lambda i: (0, 0)),
        ],
        out_specs=[
            pl.BlockSpec((block, both), lambda i: (i, 0)),
            pl.BlockSpec((block, hidden_width), lambda i: (i, 0)),
            pl.BlockSpec((block, gate_width), lambda i: (i, 0)),
        ],
        out_shape=[
            jax.ShapeDtypeStruct((slots, both), jnp.bfloat16),
            jax.ShapeDtypeStruct((slots, hidden_width), jnp.bfloat16),
            jax.ShapeDtypeStruct((slots, gate_width), jnp.bfloat16),
        ],
    )(recv, weights)


def combine_kernel(comb_ref, back_ref, cot_ref, moe_ref, tgrad_ref, gate_ref, *, width, tokens):
    contract_last = (((1,), (1,)), ((), ()))
    out_rows = back_ref[:, :width]
    weighted = jnp.dot(comb_ref[: 3 * tokens, :], out_rows, preferred_element_type=jnp.float32)
    moe_ref[...] = (
        weighted[:tokens] + weighted[tokens : 2 * tokens] + weighted[2 * tokens :]
    ).astype(moe_ref.dtype)
    tgrad_ref[...] = jnp.dot(
        comb_ref[3 * tokens :, :], back_ref[:, width:], preferred_element_type=jnp.float32
    ).astype(tgrad_ref.dtype)
    gate_ref[...] = lax.dot_general(
        cot_ref[...], out_rows, contract_last, preferred_element_type=jnp.float32
    )


def combine_call(comb_t, back, cotangent):
    tokens, width = cotangent.shape
    slots = back.shape[0]
    kernel = functools.partial(combine_kernel, width=width, tokens=tokens)
    return pl.pallas_call(
        kernel,
        out_shape=[
            jax.ShapeDtypeStruct((tokens, width), jnp.bfloat16),
            jax.ShapeDtypeStruct((tokens, width), jnp.bfloat16),
            jax.ShapeDtypeStruct((tokens, slots), jnp.float32),
        ],
    )(comb_t, back, cotangent)


def gather_dp(block):
    size = lax.axis_size("dp")
    me = lax.axis_index("dp")
    pieces = [block]
    for shift in range(1, size):
        pairs = [(i, (i + shift) % size) for i in range(size)]
        pieces.append(lax.ppermute(block, "dp", pairs))
    stacked = jnp.stack(pieces[::-1] + pieces[::-1])
    return lax.dynamic_slice_in_dim(stacked, size - 1 - me, size, axis=0).reshape(
        size * block.shape[0], block.shape[1]
    )


def scatter_dp(full):
    size = lax.axis_size("dp")
    me = lax.axis_index("dp")
    rows = full.shape[0] // size
    blocks = full.reshape(size, rows, full.shape[1])
    total = lax.dynamic_index_in_dim(blocks, me, axis=0, keepdims=False).astype(jnp.float32)
    for shift in range(1, size):
        pairs = [(i, (i + shift) % size) for i in range(size)]
        part = lax.dynamic_index_in_dim(blocks, (me + shift) % size, axis=0, keepdims=False)
        total = total + lax.ppermute(part, "dp", pairs).astype(jnp.float32)
    return total


def local(tokens, expert_ids, gate_probs, gate_up, down_proj, cotangent):
    token_count, top_count = expert_ids.shape
    width = tokens.shape[1]
    expert_count = lax.axis_size("expert")
    capacity = 2 * token_count * top_count // expert_count
    route_count = token_count * top_count
    slot_count = expert_count * capacity
    gate_width = gate_up.shape[2]

    weights = gather_dp(jnp.concatenate([gate_up[0], down_proj[0].T], axis=1))

    flat_ids = expert_ids.reshape(route_count)
    onehot = (flat_ids[:, None] == jnp.arange(expert_count, dtype=jnp.int32)[None, :]).astype(
        jnp.int32
    )
    slot_index = jnp.sum((jnp.cumsum(onehot, axis=0) - onehot) * onehot, axis=1)
    position = (flat_ids * capacity + slot_index).reshape(token_count, top_count)
    slot_range = jnp.arange(slot_count, dtype=jnp.int32)
    hits = position[None, :, :] == slot_range[:, None, None]
    select = jnp.any(hits, axis=2)
    weighted = jnp.sum(jnp.where(hits, gate_probs[None, :, :], 0.0), axis=2)
    slot_probs = jnp.sum(weighted, axis=1)
    select_rows = select.astype(jnp.bfloat16)

    both = jnp.concatenate([tokens, cotangent], axis=1)
    gathered = jnp.dot(select_rows, both, preferred_element_type=jnp.float32)
    column = lax.broadcasted_iota(jnp.int32, gathered.shape, 1)
    send = (gathered * jnp.where(column < width, 1.0, slot_probs[:, None])).astype(jnp.bfloat16)

    recv = lax.all_to_all(send, "expert", split_axis=0, concat_axis=0, tiled=True)
    payload, hidden, grad_pre = expert_call(recv, weights, gate_width)
    back = lax.all_to_all(payload, "expert", split_axis=0, concat_axis=0, tiled=True)
    contract_first = (((0,), (0,)), ((), ()))
    weight_in_grad = lax.dot_general(
        recv[:, :width], grad_pre, contract_first, preferred_element_type=jnp.float32
    ).astype(jnp.bfloat16)
    weight_out_grad_t = lax.dot_general(
        recv[:, width:], hidden, contract_first, preferred_element_type=jnp.float32
    ).astype(jnp.bfloat16)
    grads = scatter_dp(jnp.concatenate([weight_in_grad, weight_out_grad_t], axis=1))
    sum_in = grads[None, :, :gate_width]
    sum_out = grads[:, gate_width:].T[None]

    high = lax.reduce_precision(weighted, exponent_bits=8, mantissa_bits=7)
    rest = weighted - high
    middle = lax.reduce_precision(rest, exponent_bits=8, mantissa_bits=7)
    low = rest - middle
    parts = [part.astype(jnp.bfloat16) for part in (high, middle, low)]
    combine = jnp.concatenate(parts + [select_rows], axis=1)
    moe_out, token_grads, token_slot = combine_call(combine.T, back, cotangent)
    gate_grads = jnp.sum(jnp.where(hits, token_slot.T[:, :, None], 0.0), axis=0)
    return (moe_out, token_grads, gate_grads, sum_in, sum_out)


def solution(mesh):
    return jax.shard_map(
        local,
        mesh=mesh,
        in_specs=(
            P(("dp", "expert"), None),
            P(("dp", "expert"), None),
            P(("dp", "expert"), None),
            P("expert", "dp", None),
            P("expert", None, "dp"),
            P(("dp", "expert"), None),
        ),
        out_specs=(
            P(("dp", "expert"), None),
            P(("dp", "expert"), None),
            P(("dp", "expert"), None),
            P("expert", "dp", None),
            P("expert", None, "dp"),
        ),
        check_vma=False,
    )
```

```python
import functools

import jax
import jax.numpy as jnp
from jax import lax
from jax.experimental import pallas as pl
from jax.sharding import PartitionSpec as P


def expert_kernel(recv_ref, w_ref, out_ref, hid_ref, dp_ref, *, width, gate_width, hidden_width):
    contract_last = (((1,), (1,)), ((), ()))
    rows = recv_ref[:, :width]
    grads = recv_ref[:, width:]
    w_in = w_ref[:, :gate_width]
    w_out_t = w_ref[:, gate_width:]
    pre = jnp.dot(rows, w_in, preferred_element_type=jnp.float32)
    pre_gate = pre[:, :hidden_width]
    up = pre[:, hidden_width:]
    sig = 1.0 / (1.0 + jnp.exp(-pre_gate))
    act = pre_gate * sig
    hid = (act * up).astype(jnp.bfloat16)
    q = jnp.dot(grads, w_out_t, preferred_element_type=jnp.float32)
    grad_gate = q * up * sig * (1.0 + pre_gate * (1.0 - sig))
    grad_up = q * act
    dp = jnp.concatenate([grad_gate, grad_up], axis=1).astype(jnp.bfloat16)
    out_ref[:, :width] = lax.dot_general(
        hid, w_out_t, contract_last, preferred_element_type=jnp.float32
    ).astype(jnp.bfloat16)
    out_ref[:, width:] = lax.dot_general(
        dp, w_in, contract_last, preferred_element_type=jnp.float32
    ).astype(jnp.bfloat16)
    hid_ref[...] = hid
    dp_ref[...] = dp


def expert_call(recv, weights, gate_width, block=256):
    slots, both = recv.shape
    width = both // 2
    hidden_width = weights.shape[1] - gate_width
    kernel = functools.partial(
        expert_kernel, width=width, gate_width=gate_width, hidden_width=hidden_width
    )
    return pl.pallas_call(
        kernel,
        grid=(slots // block,),
        in_specs=[
            pl.BlockSpec((block, both), lambda i: (i, 0)),
            pl.BlockSpec(weights.shape, lambda i: (0, 0)),
        ],
        out_specs=[
            pl.BlockSpec((block, both), lambda i: (i, 0)),
            pl.BlockSpec((block, hidden_width), lambda i: (i, 0)),
            pl.BlockSpec((block, gate_width), lambda i: (i, 0)),
        ],
        out_shape=[
            jax.ShapeDtypeStruct((slots, both), jnp.bfloat16),
            jax.ShapeDtypeStruct((slots, hidden_width), jnp.bfloat16),
            jax.ShapeDtypeStruct((slots, gate_width), jnp.bfloat16),
        ],
    )(recv, weights)


def combine_kernel(comb_ref, back_ref, cot_ref, moe_ref, tgrad_ref, gate_ref, *, width, tokens):
    contract_last = (((1,), (1,)), ((), ()))
    out_rows = back_ref[:, :width]
    weighted = jnp.dot(comb_ref[: 3 * tokens, :], out_rows, preferred_element_type=jnp.float32)
    moe_ref[...] = (
        weighted[:tokens] + weighted[tokens : 2 * tokens] + weighted[2 * tokens :]
    ).astype(moe_ref.dtype)
    tgrad_ref[...] = jnp.dot(
        comb_ref[3 * tokens :, :], back_ref[:, width:], preferred_element_type=jnp.float32
    ).astype(tgrad_ref.dtype)
    gate_ref[...] = lax.dot_general(
        cot_ref[...], out_rows, contract_last, preferred_element_type=jnp.float32
    )


def combine_call(comb_t, back, cotangent):
    tokens, width = cotangent.shape
    slots = back.shape[0]
    kernel = functools.partial(combine_kernel, width=width, tokens=tokens)
    return pl.pallas_call(
        kernel,
        out_shape=[
            jax.ShapeDtypeStruct((tokens, width), jnp.bfloat16),
            jax.ShapeDtypeStruct((tokens, width), jnp.bfloat16),
            jax.ShapeDtypeStruct((tokens, slots), jnp.float32),
        ],
    )(comb_t, back, cotangent)


def dispatch_kernel(sel_ref, both_ref, prob_ref, send_ref, *, width):
    gathered = jnp.dot(sel_ref[...], both_ref[...], preferred_element_type=jnp.float32)
    send_ref[:, :width] = gathered[:, :width].astype(send_ref.dtype)
    send_ref[:, width:] = (gathered[:, width:] * prob_ref[...]).astype(send_ref.dtype)


def dispatch_call(select_rows, both, slot_probs, block=256):
    slots, tokens = select_rows.shape
    columns = both.shape[1]
    kernel = functools.partial(dispatch_kernel, width=columns // 2)
    return pl.pallas_call(
        kernel,
        grid=(slots // block,),
        in_specs=[
            pl.BlockSpec((block, tokens), lambda i: (i, 0)),
            pl.BlockSpec((tokens, columns), lambda i: (0, 0)),
            pl.BlockSpec((block, 1), lambda i: (i, 0)),
        ],
        out_specs=pl.BlockSpec((block, columns), lambda i: (i, 0)),
        out_shape=jax.ShapeDtypeStruct((slots, columns), jnp.bfloat16),
    )(select_rows, both, slot_probs[:, None])


def gather_dp(block):
    size = lax.axis_size("dp")
    me = lax.axis_index("dp")
    pieces = [block]
    for shift in range(1, size):
        pairs = [(i, (i + shift) % size) for i in range(size)]
        pieces.append(lax.ppermute(block, "dp", pairs))
    stacked = jnp.stack(pieces[::-1] + pieces[::-1])
    return lax.dynamic_slice_in_dim(stacked, size - 1 - me, size, axis=0).reshape(
        size * block.shape[0], block.shape[1]
    )


def scatter_dp(full):
    size = lax.axis_size("dp")
    me = lax.axis_index("dp")
    rows = full.shape[0] // size
    blocks = full.reshape(size, rows, full.shape[1])
    total = lax.dynamic_index_in_dim(blocks, me, axis=0, keepdims=False).astype(jnp.float32)
    for shift in range(1, size):
        pairs = [(i, (i + shift) % size) for i in range(size)]
        part = lax.dynamic_index_in_dim(blocks, (me + shift) % size, axis=0, keepdims=False)
        total = total + lax.ppermute(part, "dp", pairs).astype(jnp.float32)
    return total


def local(tokens, expert_ids, gate_probs, gate_up, down_proj, cotangent):
    token_count, top_count = expert_ids.shape
    width = tokens.shape[1]
    expert_count = lax.axis_size("expert")
    capacity = 2 * token_count * top_count // expert_count
    route_count = token_count * top_count
    slot_count = expert_count * capacity
    gate_width = gate_up.shape[2]

    weights = gather_dp(jnp.concatenate([gate_up[0], down_proj[0].T], axis=1))

    flat_ids = expert_ids.reshape(route_count)
    onehot = (flat_ids[:, None] == jnp.arange(expert_count, dtype=jnp.int32)[None, :]).astype(
        jnp.int32
    )
    slot_index = jnp.sum((jnp.cumsum(onehot, axis=0) - onehot) * onehot, axis=1)
    position = (flat_ids * capacity + slot_index).reshape(token_count, top_count)
    slot_range = jnp.arange(slot_count, dtype=jnp.int32)
    hits = position[None, :, :] == slot_range[:, None, None]
    select = jnp.any(hits, axis=2)
    weighted = jnp.sum(jnp.where(hits, gate_probs[None, :, :], 0.0), axis=2)
    slot_probs = jnp.sum(weighted, axis=1)
    select_rows = select.astype(jnp.bfloat16)

    both = jnp.concatenate([tokens, cotangent], axis=1)
    send = dispatch_call(select_rows, both, slot_probs)
    recv = lax.all_to_all(send, "expert", split_axis=0, concat_axis=0, tiled=True)
    payload, hidden, grad_pre = expert_call(recv, weights, gate_width)
    back = lax.all_to_all(payload, "expert", split_axis=0, concat_axis=0, tiled=True)
    contract_first = (((0,), (0,)), ((), ()))
    weight_in_grad = lax.dot_general(
        recv[:, :width], grad_pre, contract_first, preferred_element_type=jnp.float32
    ).astype(jnp.bfloat16)
    weight_out_grad_t = lax.dot_general(
        recv[:, width:], hidden, contract_first, preferred_element_type=jnp.float32
    ).astype(jnp.bfloat16)
    grads = scatter_dp(jnp.concatenate([weight_in_grad, weight_out_grad_t], axis=1))
    sum_in = grads[None, :, :gate_width]
    sum_out = grads[:, gate_width:].T[None]

    high = lax.reduce_precision(weighted, exponent_bits=8, mantissa_bits=7)
    rest = weighted - high
    middle = lax.reduce_precision(rest, exponent_bits=8, mantissa_bits=7)
    low = rest - middle
    parts = [part.astype(jnp.bfloat16) for part in (high, middle, low)]
    combine = jnp.concatenate(parts + [select_rows], axis=1)
    moe_out, token_grads, token_slot = combine_call(combine.T, back, cotangent)
    gate_grads = jnp.sum(jnp.where(hits, token_slot.T[:, :, None], 0.0), axis=0)
    return (moe_out, token_grads, gate_grads, sum_in, sum_out)


def solution(mesh):
    return jax.shard_map(
        local,
        mesh=mesh,
        in_specs=(
            P(("dp", "expert"), None),
            P(("dp", "expert"), None),
            P(("dp", "expert"), None),
            P("expert", "dp", None),
            P("expert", None, "dp"),
            P(("dp", "expert"), None),
        ),
        out_specs=(
            P(("dp", "expert"), None),
            P(("dp", "expert"), None),
            P(("dp", "expert"), None),
            P("expert", "dp", None),
            P("expert", None, "dp"),
        ),
        check_vma=False,
    )
```

```python
import functools

import jax
import jax.numpy as jnp
from jax import lax
from jax.experimental import pallas as pl
from jax.sharding import PartitionSpec as P


def expert_kernel(recv_ref, w_ref, out_ref, hid_ref, dp_ref, *, width, gate_width, hidden_width):
    contract_last = (((1,), (1,)), ((), ()))
    rows = recv_ref[:, :width]
    grads = recv_ref[:, width:]
    w_in = w_ref[:, :gate_width]
    w_out_t = w_ref[:, gate_width:]
    pre = jnp.dot(rows, w_in, preferred_element_type=jnp.float32)
    pre_gate = pre[:, :hidden_width]
    up = pre[:, hidden_width:]
    sig = 1.0 / (1.0 + jnp.exp(-pre_gate))
    act = pre_gate * sig
    hid = (act * up).astype(jnp.bfloat16)
    q = jnp.dot(grads, w_out_t, preferred_element_type=jnp.float32)
    grad_gate = q * up * sig * (1.0 + pre_gate * (1.0 - sig))
    grad_up = q * act
    dp = jnp.concatenate([grad_gate, grad_up], axis=1).astype(jnp.bfloat16)
    out_ref[:, :width] = lax.dot_general(
        hid, w_out_t, contract_last, preferred_element_type=jnp.float32
    ).astype(jnp.bfloat16)
    out_ref[:, width:] = lax.dot_general(
        dp, w_in, contract_last, preferred_element_type=jnp.float32
    ).astype(jnp.bfloat16)
    hid_ref[...] = hid
    dp_ref[...] = dp


def expert_call(recv, weights, gate_width, block=512):
    slots, both = recv.shape
    width = both // 2
    hidden_width = weights.shape[1] - gate_width
    kernel = functools.partial(
        expert_kernel, width=width, gate_width=gate_width, hidden_width=hidden_width
    )
    return pl.pallas_call(
        kernel,
        grid=(slots // block,),
        in_specs=[
            pl.BlockSpec((block, both), lambda i: (i, 0)),
            pl.BlockSpec(weights.shape, lambda i: (0, 0)),
        ],
        out_specs=[
            pl.BlockSpec((block, both), lambda i: (i, 0)),
            pl.BlockSpec((block, hidden_width), lambda i: (i, 0)),
            pl.BlockSpec((block, gate_width), lambda i: (i, 0)),
        ],
        out_shape=[
            jax.ShapeDtypeStruct((slots, both), jnp.bfloat16),
            jax.ShapeDtypeStruct((slots, hidden_width), jnp.bfloat16),
            jax.ShapeDtypeStruct((slots, gate_width), jnp.bfloat16),
        ],
    )(recv, weights)


def combine_kernel(comb_ref, back_ref, cot_ref, moe_ref, tgrad_ref, gate_ref, *, width, tokens):
    contract_last = (((1,), (1,)), ((), ()))
    out_rows = back_ref[:, :width]
    weighted = jnp.dot(comb_ref[: 3 * tokens, :], out_rows, preferred_element_type=jnp.float32)
    moe_ref[...] = (
        weighted[:tokens] + weighted[tokens : 2 * tokens] + weighted[2 * tokens :]
    ).astype(moe_ref.dtype)
    tgrad_ref[...] = jnp.dot(
        comb_ref[3 * tokens :, :], back_ref[:, width:], preferred_element_type=jnp.float32
    ).astype(tgrad_ref.dtype)
    gate_ref[...] = lax.dot_general(
        cot_ref[...], out_rows, contract_last, preferred_element_type=jnp.float32
    )


def combine_call(comb_t, back, cotangent):
    tokens, width = cotangent.shape
    slots = back.shape[0]
    kernel = functools.partial(combine_kernel, width=width, tokens=tokens)
    return pl.pallas_call(
        kernel,
        out_shape=[
            jax.ShapeDtypeStruct((tokens, width), jnp.bfloat16),
            jax.ShapeDtypeStruct((tokens, width), jnp.bfloat16),
            jax.ShapeDtypeStruct((tokens, slots), jnp.float32),
        ],
    )(comb_t, back, cotangent)


def gather_dp(block):
    size = lax.axis_size("dp")
    me = lax.axis_index("dp")
    pieces = [block]
    for shift in range(1, size):
        pairs = [(i, (i + shift) % size) for i in range(size)]
        pieces.append(lax.ppermute(block, "dp", pairs))
    stacked = jnp.stack(pieces[::-1] + pieces[::-1])
    return lax.dynamic_slice_in_dim(stacked, size - 1 - me, size, axis=0).reshape(
        size * block.shape[0], block.shape[1]
    )


def scatter_dp(full):
    size = lax.axis_size("dp")
    me = lax.axis_index("dp")
    rows = full.shape[0] // size
    blocks = full.reshape(size, rows, full.shape[1])
    total = lax.dynamic_index_in_dim(blocks, me, axis=0, keepdims=False).astype(jnp.float32)
    for shift in range(1, size):
        pairs = [(i, (i + shift) % size) for i in range(size)]
        part = lax.dynamic_index_in_dim(blocks, (me + shift) % size, axis=0, keepdims=False)
        total = total + lax.ppermute(part, "dp", pairs).astype(jnp.float32)
    return total


def local(tokens, expert_ids, gate_probs, gate_up, down_proj, cotangent):
    token_count, top_count = expert_ids.shape
    width = tokens.shape[1]
    expert_count = lax.axis_size("expert")
    capacity = 2 * token_count * top_count // expert_count
    route_count = token_count * top_count
    slot_count = expert_count * capacity
    gate_width = gate_up.shape[2]

    weights = gather_dp(jnp.concatenate([gate_up[0], down_proj[0].T], axis=1))

    flat_ids = expert_ids.reshape(route_count)
    onehot = (flat_ids[:, None] == jnp.arange(expert_count, dtype=jnp.int32)[None, :]).astype(
        jnp.int32
    )
    slot_index = jnp.sum((jnp.cumsum(onehot, axis=0) - onehot) * onehot, axis=1)
    position = (flat_ids * capacity + slot_index).reshape(token_count, top_count)
    slot_range = jnp.arange(slot_count, dtype=jnp.int32)
    hits = position[None, :, :] == slot_range[:, None, None]
    select = jnp.any(hits, axis=2)
    weighted = jnp.sum(jnp.where(hits, gate_probs[None, :, :], 0.0), axis=2)
    slot_probs = jnp.sum(weighted, axis=1)
    select_rows = select.astype(jnp.bfloat16)

    both = jnp.concatenate([tokens, cotangent], axis=1)
    gathered = jnp.dot(select_rows, both, preferred_element_type=jnp.float32)
    column = lax.broadcasted_iota(jnp.int32, gathered.shape, 1)
    send = (gathered * jnp.where(column < width, 1.0, slot_probs[:, None])).astype(jnp.bfloat16)

    recv = lax.all_to_all(send, "expert", split_axis=0, concat_axis=0, tiled=True)
    payload, hidden, grad_pre = expert_call(recv, weights, gate_width)
    back = lax.all_to_all(payload, "expert", split_axis=0, concat_axis=0, tiled=True)
    contract_first = (((0,), (0,)), ((), ()))
    weight_in_grad = lax.dot_general(
        recv[:, :width], grad_pre, contract_first, preferred_element_type=jnp.float32
    ).astype(jnp.bfloat16)
    weight_out_grad_t = lax.dot_general(
        recv[:, width:], hidden, contract_first, preferred_element_type=jnp.float32
    ).astype(jnp.bfloat16)
    grads = scatter_dp(jnp.concatenate([weight_in_grad, weight_out_grad_t], axis=1))
    sum_in = grads[None, :, :gate_width]
    sum_out = grads[:, gate_width:].T[None]

    high = lax.reduce_precision(weighted, exponent_bits=8, mantissa_bits=7)
    rest = weighted - high
    middle = lax.reduce_precision(rest, exponent_bits=8, mantissa_bits=7)
    low = rest - middle
    parts = [part.astype(jnp.bfloat16) for part in (high, middle, low)]
    combine = jnp.concatenate(parts + [select_rows], axis=1)
    moe_out, token_grads, token_slot = combine_call(combine.T, back, cotangent)
    gate_grads = jnp.sum(jnp.where(hits, token_slot.T[:, :, None], 0.0), axis=0)
    return (moe_out, token_grads, gate_grads, sum_in, sum_out)


def solution(mesh):
    return jax.shard_map(
        local,
        mesh=mesh,
        in_specs=(
            P(("dp", "expert"), None),
            P(("dp", "expert"), None),
            P(("dp", "expert"), None),
            P("expert", "dp", None),
            P("expert", None, "dp"),
            P(("dp", "expert"), None),
        ),
        out_specs=(
            P(("dp", "expert"), None),
            P(("dp", "expert"), None),
            P(("dp", "expert"), None),
            P("expert", "dp", None),
            P("expert", None, "dp"),
        ),
        check_vma=False,
    )
```

```python
import functools

import jax
import jax.numpy as jnp
from jax import lax
from jax.experimental import pallas as pl
from jax.sharding import PartitionSpec as P


def expert_kernel(recv_ref, w_ref, out_ref, hid_ref, dp_ref, *, width, gate_width, hidden_width):
    contract_last = (((1,), (1,)), ((), ()))
    rows = recv_ref[:, :width]
    grads = recv_ref[:, width:]
    w_in = w_ref[:, :gate_width]
    w_out_t = w_ref[:, gate_width:]
    pre = jnp.dot(rows, w_in, preferred_element_type=jnp.float32)
    pre_gate = pre[:, :hidden_width]
    up = pre[:, hidden_width:]
    sig = 1.0 / (1.0 + jnp.exp(-pre_gate))
    act = pre_gate * sig
    hid = (act * up).astype(jnp.bfloat16)
    q = jnp.dot(grads, w_out_t, preferred_element_type=jnp.float32)
    grad_gate = q * up * sig * (1.0 + pre_gate * (1.0 - sig))
    grad_up = q * act
    dp = jnp.concatenate([grad_gate, grad_up], axis=1).astype(jnp.bfloat16)
    out_ref[:, :width] = lax.dot_general(
        hid, w_out_t, contract_last, preferred_element_type=jnp.float32
    ).astype(jnp.bfloat16)
    out_ref[:, width:] = lax.dot_general(
        dp, w_in, contract_last, preferred_element_type=jnp.float32
    ).astype(jnp.bfloat16)
    hid_ref[...] = hid
    dp_ref[...] = dp


def expert_call(recv, weights, gate_width, block=512):
    slots, both = recv.shape
    width = both // 2
    hidden_width = weights.shape[1] - gate_width
    kernel = functools.partial(
        expert_kernel, width=width, gate_width=gate_width, hidden_width=hidden_width
    )
    return pl.pallas_call(
        kernel,
        grid=(slots // block,),
        in_specs=[
            pl.BlockSpec((block, both), lambda i: (i, 0)),
            pl.BlockSpec(weights.shape, lambda i: (0, 0)),
        ],
        out_specs=[
            pl.BlockSpec((block, both), lambda i: (i, 0)),
            pl.BlockSpec((block, hidden_width), lambda i: (i, 0)),
            pl.BlockSpec((block, gate_width), lambda i: (i, 0)),
        ],
        out_shape=[
            jax.ShapeDtypeStruct((slots, both), jnp.bfloat16),
            jax.ShapeDtypeStruct((slots, hidden_width), jnp.bfloat16),
            jax.ShapeDtypeStruct((slots, gate_width), jnp.bfloat16),
        ],
    )(recv, weights)


def combine_kernel(comb_ref, back_ref, cot_ref, moe_ref, tgrad_ref, gate_ref, *, width, tokens):
    contract_last = (((1,), (1,)), ((), ()))
    out_rows = back_ref[:, :width]
    weighted = jnp.dot(comb_ref[: 3 * tokens, :], out_rows, preferred_element_type=jnp.float32)
    moe_ref[...] = (
        weighted[:tokens] + weighted[tokens : 2 * tokens] + weighted[2 * tokens :]
    ).astype(moe_ref.dtype)
    tgrad_ref[...] = jnp.dot(
        comb_ref[3 * tokens :, :], back_ref[:, width:], preferred_element_type=jnp.float32
    ).astype(tgrad_ref.dtype)
    gate_ref[...] = lax.dot_general(
        cot_ref[...], out_rows, contract_last, preferred_element_type=jnp.float32
    )


def combine_call(comb_t, back, cotangent):
    tokens, width = cotangent.shape
    slots = back.shape[0]
    kernel = functools.partial(combine_kernel, width=width, tokens=tokens)
    return pl.pallas_call(
        kernel,
        out_shape=[
            jax.ShapeDtypeStruct((tokens, width), jnp.bfloat16),
            jax.ShapeDtypeStruct((tokens, width), jnp.bfloat16),
            jax.ShapeDtypeStruct((tokens, slots), jnp.float32),
        ],
    )(comb_t, back, cotangent)


def gather_dp(block):
    size = lax.axis_size("dp")
    me = lax.axis_index("dp")
    pieces = [block]
    for shift in range(1, size):
        pairs = [(i, (i + shift) % size) for i in range(size)]
        pieces.append(lax.ppermute(block, "dp", pairs))
    stacked = jnp.stack(pieces[::-1] + pieces[::-1])
    return lax.dynamic_slice_in_dim(stacked, size - 1 - me, size, axis=0).reshape(
        size * block.shape[0], block.shape[1]
    )


def scatter_dp(full):
    size = lax.axis_size("dp")
    me = lax.axis_index("dp")
    rows = full.shape[0] // size
    blocks = full.reshape(size, rows, full.shape[1])
    total = lax.dynamic_index_in_dim(blocks, me, axis=0, keepdims=False).astype(jnp.float32)
    for shift in range(1, size):
        pairs = [(i, (i + shift) % size) for i in range(size)]
        part = lax.dynamic_index_in_dim(blocks, (me + shift) % size, axis=0, keepdims=False)
        total = total + lax.ppermute(part, "dp", pairs).astype(jnp.float32)
    return total


def local(tokens, expert_ids, gate_probs, gate_up, down_proj, cotangent):
    token_count, top_count = expert_ids.shape
    width = tokens.shape[1]
    expert_count = lax.axis_size("expert")
    capacity = 2 * token_count * top_count // expert_count
    route_count = token_count * top_count
    slot_count = expert_count * capacity
    gate_width = gate_up.shape[2]

    weights = gather_dp(jnp.concatenate([gate_up[0], down_proj[0].T], axis=1))

    flat_ids = expert_ids.reshape(route_count)
    onehot = (flat_ids[:, None] == jnp.arange(expert_count, dtype=jnp.int32)[None, :]).astype(
        jnp.int32
    )
    earlier = lax.broadcasted_iota(jnp.int32, (route_count, route_count), 1) < lax.broadcasted_iota(
        jnp.int32, (route_count, route_count), 0
    )
    before = jnp.dot(
        earlier.astype(jnp.bfloat16), onehot.astype(jnp.bfloat16), preferred_element_type=jnp.float32
    ).astype(jnp.int32)
    slot_index = jnp.sum(before * onehot, axis=1)
    position = (flat_ids * capacity + slot_index).reshape(token_count, top_count)
    slot_range = jnp.arange(slot_count, dtype=jnp.int32)
    hits = position[None, :, :] == slot_range[:, None, None]
    select = jnp.any(hits, axis=2)
    weighted = jnp.sum(jnp.where(hits, gate_probs[None, :, :], 0.0), axis=2)
    slot_probs = jnp.sum(weighted, axis=1)
    select_rows = select.astype(jnp.bfloat16)

    both = jnp.concatenate([tokens, cotangent], axis=1)
    gathered = jnp.dot(select_rows, both, preferred_element_type=jnp.float32)
    column = lax.broadcasted_iota(jnp.int32, gathered.shape, 1)
    send = (gathered * jnp.where(column < width, 1.0, slot_probs[:, None])).astype(jnp.bfloat16)

    recv = lax.all_to_all(send, "expert", split_axis=0, concat_axis=0, tiled=True)
    payload, hidden, grad_pre = expert_call(recv, weights, gate_width)
    back = lax.all_to_all(payload, "expert", split_axis=0, concat_axis=0, tiled=True)
    contract_first = (((0,), (0,)), ((), ()))
    weight_in_grad = lax.dot_general(
        recv[:, :width], grad_pre, contract_first, preferred_element_type=jnp.float32
    ).astype(jnp.bfloat16)
    weight_out_grad_t = lax.dot_general(
        recv[:, width:], hidden, contract_first, preferred_element_type=jnp.float32
    ).astype(jnp.bfloat16)
    grads = scatter_dp(jnp.concatenate([weight_in_grad, weight_out_grad_t], axis=1))
    sum_in = grads[None, :, :gate_width]
    sum_out = grads[:, gate_width:].T[None]

    high = lax.reduce_precision(weighted, exponent_bits=8, mantissa_bits=7)
    rest = weighted - high
    middle = lax.reduce_precision(rest, exponent_bits=8, mantissa_bits=7)
    low = rest - middle
    parts = [part.astype(jnp.bfloat16) for part in (high, middle, low)]
    combine = jnp.concatenate(parts + [select_rows], axis=1)
    moe_out, token_grads, token_slot = combine_call(combine.T, back, cotangent)
    gate_grads = jnp.sum(jnp.where(hits, token_slot.T[:, :, None], 0.0), axis=0)
    return (moe_out, token_grads, gate_grads, sum_in, sum_out)


def solution(mesh):
    return jax.shard_map(
        local,
        mesh=mesh,
        in_specs=(
            P(("dp", "expert"), None),
            P(("dp", "expert"), None),
            P(("dp", "expert"), None),
            P("expert", "dp", None),
            P("expert", None, "dp"),
            P(("dp", "expert"), None),
        ),
        out_specs=(
            P(("dp", "expert"), None),
            P(("dp", "expert"), None),
            P(("dp", "expert"), None),
            P("expert", "dp", None),
            P("expert", None, "dp"),
        ),
        check_vma=False,
    )
```
